512 devices in a mesh: box: 8 (over z_lo, core), panel: 64 (over y, x, z_hi).
Axes of the slice: x: 4, y: 4, z: 16 (z_hi: 4, z_lo: 4; z = z_hi * 4 + z_lo), core: 2. Of those that a mesh axis runs over, the one named last changes fastest.
Arguments:
- exterior_rows: float32 [8, 2048, 2, 128], P('box'), may hold values from -6 to 6
- exterior_block: float32 [8, 6144, 2, 128], P('box', 'panel'), may hold values from -6 to 6
- shared_block: float32 [8, 2048, 2, 2048], P('box', 'panel'), may hold values from -0.9 to 0.9
- crossing_block: float32 [8, 6144, 2, 2048], P('box', 'panel'), may hold values from -0.125 to 0.125
Outputs:
- merged_map: float32 [8, 2, 6144, 2, 128], P('box', None, 'panel')
The draws below stay inside these ranges and needn't reach their ends.
All inputs are finite; a program needn't handle non-finite values.
Results may differ from the reference program's by a relative error of at most 0.0001.
Values sent between devices are 32-bit elements; how exact they have to be, the bound alone decides.
No kernel may reach another device: no remote copies, remote signals or barrier semaphores. Data moves between devices by JAX's collectives and lax.ppermute only.
A program may use at most 64 MiB of HBM per device.

```python
import math
import jax
import jax.numpy as jnp
from jax import lax

SHARED = 2048
OUTER = 6144
ROWS = 128
ITERS = 3
BOXES = 8


def draw_shared_block(key, part):
    key_mag, key_phase, key_off = jax.random.split(key, 3)
    magnitude = jax.random.uniform(key_mag, (BOXES, SHARED), jnp.float32, 0.4, 0.85)
    phase = jax.random.uniform(key_phase, (BOXES, SHARED), jnp.float32, -math.pi, math.pi)
    diagonal = jnp.stack([magnitude * jnp.cos(phase), magnitude * jnp.sin(phase)], axis=-1)[:, :, :, None]
    spread = 0.15 / math.sqrt(SHARED)
    off_part = jnp.clip(jax.random.normal(key_off, (BOXES, SHARED, 2, SHARED), jnp.float32), -6.0, 6.0) * spread
    column_ids = jnp.arange(SHARED, dtype=jnp.int32)[:, None, None]
    row_ids = jnp.arange(SHARED, dtype=jnp.int32)[None, None, :]
    on_diagonal = (column_ids == row_ids).astype(jnp.float32)[None]
    return off_part * (1.0 - on_diagonal) + on_diagonal * diagonal


def level_of(stream_key, shape, shards, least, high):
    level, own = 1.0, jax.random.fold_in(stream_key, 6)
    for dim, parts in shards:
        draws = jnp.exp(jax.random.uniform(jax.random.fold_in(own, dim), (parts,), jnp.float32, least / len(shards), high / len(shards)))
        level = level * jnp.repeat(draws, shape[dim] // parts).reshape([-1 if axis == dim else 1 for axis in range(len(shape))])
    return level


def scatter_about(own_key, shape, scale, most, cuts=(), held_as=jnp.bfloat16):
    level = level_of(own_key, shape, cuts, -0.22, 0.18) if cuts else 1.0
    entries = jax.random.normal(own_key, shape, jnp.float32) * scale * level
    return jnp.minimum(jnp.maximum(entries, -most), most).astype(held_as)


def setup_inputs(seed: int = 0) -> dict:
    key_of = jax.random.split(jax.random.key(seed), 5)
    exterior_rows = scatter_about(key_of[0], (BOXES, SHARED, 2, ROWS), 1.0, 6.0, ((0, 8),), jnp.float32)
    exterior_block = scatter_about(key_of[1], (BOXES, OUTER, 2, ROWS), 1.0, 6.0, ((0, 8), (1, 64)), jnp.float32)
    shared_block = draw_shared_block(jax.random.fold_in(key_of[4], 71), 0)
    crossing_block = scatter_about(key_of[3], (BOXES, OUTER, 2, SHARED), SHARED ** -0.5, 0.125, ((0, 8), (1, 64)), jnp.float32)
    return dict(exterior_rows=exterior_rows, exterior_block=exterior_block, shared_block=shared_block, crossing_block=crossing_block)


def complex_product(left_factor, operand):
    highest = lax.Precision.HIGHEST
    real_part = jnp.dot(left_factor[:, 0], operand[:, 0], precision=highest, preferred_element_type=jnp.float32) - jnp.dot(left_factor[:, 1], operand[:, 1], precision=highest, preferred_element_type=jnp.float32)
    imag_part = jnp.dot(left_factor[:, 0], operand[:, 1], precision=highest, preferred_element_type=jnp.float32) + jnp.dot(left_factor[:, 1], operand[:, 0], precision=highest, preferred_element_type=jnp.float32)
    return jnp.stack([real_part, imag_part], axis=1)


def sibling_of(stacked):
    full_shape = stacked.shape
    paired = stacked.reshape((full_shape[0] // 2, 2) + full_shape[1:])
    return paired[:, ::-1].reshape(full_shape)


def reference(exterior_rows, exterior_block, shared_block, crossing_block):
    sibling_shared = sibling_of(shared_block)
    sibling_crossing = sibling_of(crossing_block)
    results = []
    for member in range(BOXES):
        own_shared = shared_block[member]
        other_shared = sibling_shared[member]
        start_rows = exterior_rows[member]
        rows_now = start_rows
        for iteration in range(ITERS):
            image_now = complex_product(other_shared, rows_now)
            rows_now = start_rows + complex_product(own_shared, image_now)
        image_now = complex_product(other_shared, rows_now)
        own_part = exterior_block[member] + complex_product(crossing_block[member], image_now)
        other_part = -complex_product(sibling_crossing[member], rows_now)
        results.append(jnp.stack([own_part, other_part], axis=0))
    return jnp.stack(results, axis=0)
```

```python
import jax
import jax.numpy as jnp
from jax import lax
from jax.sharding import PartitionSpec as P

ITERS = 3


def swapped(shard, axis, bit):
    return lax.ppermute(shard, axis, [(i, i ^ 1 << bit) for i in range(lax.axis_size(axis))])


def complex_product(left_factor, operand):
    highest = lax.Precision.HIGHEST
    real_part = jnp.dot(
        left_factor[:, 0], operand[:, 0], precision=highest, preferred_element_type=jnp.float32
    ) - jnp.dot(
        left_factor[:, 1], operand[:, 1], precision=highest, preferred_element_type=jnp.float32
    )
    imag_part = jnp.dot(
        left_factor[:, 0], operand[:, 1], precision=highest, preferred_element_type=jnp.float32
    ) + jnp.dot(
        left_factor[:, 1], operand[:, 0], precision=highest, preferred_element_type=jnp.float32
    )
    return jnp.stack([real_part, imag_part], axis=1)


def ring_stage(piece, stride):
    count = lax.axis_size("panel")
    digit = (lax.axis_index("panel") // stride) % 4
    pieces = [piece]
    for shift in (1, 2, 3):
        pairs = []
        for source in range(count):
            own = (source // stride) % 4
            pairs.append((source, source + ((own + shift) % 4 - own) * stride))
        pieces.append(lax.ppermute(piece, "panel", pairs))
    stacked = jnp.stack(pieces, 0)
    order = (digit - jnp.arange(4)) % 4
    out = jnp.take(stacked, order, axis=0)
    return out.reshape((4 * piece.shape[0],) + piece.shape[1:])


def panel_gather(piece):
    for stride in (1, 4, 16):
        piece = ring_stage(piece, stride)
    return piece


def slice_product(matrix, gathered_piece):
    return complex_product(matrix, gathered_piece)


def local(exterior_rows, exterior_block, shared_block, crossing_block):
    start_rows = exterior_rows[0]
    own_exterior = exterior_block[0]
    own_shared = shared_block[0]
    own_crossing = crossing_block[0]
    width_panel = own_shared.shape[0]
    panel_index = lax.axis_index("panel")
    own_rows = lax.dynamic_slice_in_dim(start_rows, panel_index * width_panel, width_panel, 0)
    other_form, other_crossing = swapped((own_shared, own_crossing), "box", 0)

    def through_own(gathered_piece):
        return slice_product(own_shared, gathered_piece)

    def own_step(image_now):
        return own_rows + through_own(panel_gather(image_now))

    image_panel = complex_product(other_form, start_rows)
    rows_panel = own_step(image_panel)
    for iteration in range(1, ITERS):
        image_panel = slice_product(
            other_form, panel_gather(rows_panel)
        )
        rows_panel = own_step(image_panel)
    gathered_piece = panel_gather(rows_panel)
    image_final = slice_product(other_form, gathered_piece)
    other_terms = slice_product(other_crossing, gathered_piece)
    own_terms = slice_product(
        own_crossing, panel_gather(image_final)
    )
    merged = jnp.stack([own_exterior + own_terms, -other_terms], axis=0)
    return merged[None]


def solution(mesh):
    return jax.shard_map(
        local,
        mesh=mesh,
        in_specs=(
            P("box", None, None, None),
            P("box", "panel", None, None),
            P("box", "panel", None, None),
            P("box", "panel", None, None),
        ),
        out_specs=P("box", None, "panel", None, None),
        check_vma=False,
    )
```

```python
import jax
import jax.numpy as jnp
from jax import lax
from jax.sharding import PartitionSpec as P

ITERS = 3


def swapped(shard, axis, bit):
    return lax.ppermute(shard, axis, [(i, i ^ 1 << bit) for i in range(lax.axis_size(axis))])


def complex_product(left_factor, operand):
    highest = lax.Precision.HIGHEST
    real_part = jnp.dot(
        left_factor[:, 0], operand[:, 0], precision=highest, preferred_element_type=jnp.float32
    ) - jnp.dot(
        left_factor[:, 1], operand[:, 1], precision=highest, preferred_element_type=jnp.float32
    )
    imag_part = jnp.dot(
        left_factor[:, 0], operand[:, 1], precision=highest, preferred_element_type=jnp.float32
    ) + jnp.dot(
        left_factor[:, 1], operand[:, 0], precision=highest, preferred_element_type=jnp.float32
    )
    return jnp.stack([real_part, imag_part], axis=1)


def shifted_along(piece, stride, shift):
    pairs = []
    for source in range(lax.axis_size("panel")):
        own = (source // stride) % 4
        pairs.append((source, source + ((own + shift) % 4 - own) * stride))
    return lax.ppermute(piece, "panel", pairs)


def direct_stage(blocks, stride):
    return jnp.stack(
        [blocks, shifted_along(blocks, stride, 3), shifted_along(blocks, stride, 2),
         shifted_along(blocks, stride, 1)], 0)


def relay_stage(blocks, stride):
    from_below = shifted_along(blocks, stride, 1)
    from_above = shifted_along(blocks, stride, 3)
    half = blocks.shape[0] // 2
    opposite = jnp.concatenate(
        [shifted_along(from_below[:half], stride, 1), shifted_along(from_above[half:], stride, 3)], 0)
    return jnp.stack([blocks, from_above, opposite, from_below], 0)


def panel_gather(piece):
    blocks = direct_stage(piece[None], 1)
    blocks = relay_stage(blocks, 4)
    blocks = relay_stage(blocks, 16)
    blocks = blocks.reshape((64,) + piece.shape)
    me = lax.axis_index("panel")
    target = jnp.arange(64)
    slot = jnp.zeros((64,), jnp.int32)
    for stride in (16, 4, 1):
        offset = (target // stride % 4 - me // stride % 4) % 4
        slot = slot + offset * stride
    out = jnp.take(blocks, slot, axis=0)
    return out.reshape((64 * piece.shape[0],) + piece.shape[1:])


def slice_product(matrix, gathered_piece):
    return complex_product(matrix, gathered_piece)


def local(exterior_rows, exterior_block, shared_block, crossing_block):
    start_rows = exterior_rows[0]
    own_exterior = exterior_block[0]
    own_shared = shared_block[0]
    own_crossing = crossing_block[0]
    width_panel = own_shared.shape[0]
    panel_index = lax.axis_index("panel")
    own_rows = lax.dynamic_slice_in_dim(start_rows, panel_index * width_panel, width_panel, 0)
    other_form, other_crossing = swapped((own_shared, own_crossing), "box", 0)

    def through_own(gathered_piece):
        return slice_product(own_shared, gathered_piece)

    def own_step(image_now):
        return own_rows + through_own(panel_gather(image_now))

    image_panel = complex_product(other_form, start_rows)
    rows_panel = own_step(image_panel)
    for iteration in range(1, ITERS):
        image_panel = slice_product(
            other_form, panel_gather(rows_panel)
        )
        rows_panel = own_step(image_panel)
    gathered_piece = panel_gather(rows_panel)
    image_final = slice_product(other_form, gathered_piece)
    other_terms = slice_product(other_crossing, gathered_piece)
    own_terms = slice_product(
        own_crossing, panel_gather(image_final)
    )
    merged = jnp.stack([own_exterior + own_terms, -other_terms], axis=0)
    return merged[None]


def solution(mesh):
    return jax.shard_map(
        local,
        mesh=mesh,
        in_specs=(
            P("box", None, None, None),
            P("box", "panel", None, None),
            P("box", "panel", None, None),
            P("box", "panel", None, None),
        ),
        out_specs=P("box", None, "panel", None, None),
        check_vma=False,
    )
```

```python
import jax
import jax.numpy as jnp
from jax import lax
from jax.sharding import PartitionSpec as P

ITERS = 3


def swapped(shard, axis, bit):
    return lax.ppermute(shard, axis, [(i, i ^ 1 << bit) for i in range(lax.axis_size(axis))])


def complex_product(left_factor, operand):
    highest = lax.Precision.HIGHEST
    real_part = jnp.dot(
        left_factor[:, 0], operand[:, 0], precision=highest, preferred_element_type=jnp.float32
    ) - jnp.dot(
        left_factor[:, 1], operand[:, 1], precision=highest, preferred_element_type=jnp.float32
    )
    imag_part = jnp.dot(
        left_factor[:, 0], operand[:, 1], precision=highest, preferred_element_type=jnp.float32
    ) + jnp.dot(
        left_factor[:, 1], operand[:, 0], precision=highest, preferred_element_type=jnp.float32
    )
    return jnp.stack([real_part, imag_part], axis=1)


def shifted_along(piece, stride, shift):
    pairs = []
    for source in range(lax.axis_size("panel")):
        own = (source // stride) % 4
        pairs.append((source, source + ((own + shift) % 4 - own) * stride))
    return lax.ppermute(piece, "panel", pairs)


def direct_stage(blocks, stride):
    return jnp.stack(
        [blocks, shifted_along(blocks, stride, 3), shifted_along(blocks, stride, 2),
         shifted_along(blocks, stride, 1)], 0)


def relay_stage(blocks, stride):
    from_below = shifted_along(blocks, stride, 1)
    from_above = shifted_along(blocks, stride, 3)
    half = blocks.shape[0] // 2
    opposite = jnp.concatenate(
        [shifted_along(from_below[:half], stride, 1), shifted_along(from_above[half:], stride, 3)], 0)
    return jnp.stack([blocks, from_above, opposite, from_below], 0)


def panel_gather(piece):
    blocks = direct_stage(piece[None], 1)
    blocks = direct_stage(blocks, 4)
    blocks = relay_stage(blocks, 16)
    blocks = blocks.reshape((64,) + piece.shape)
    me = lax.axis_index("panel")
    target = jnp.arange(64)
    slot = jnp.zeros((64,), jnp.int32)
    for stride in (16, 4, 1):
        offset = (target // stride % 4 - me // stride % 4) % 4
        slot = slot + offset * stride
    out = jnp.take(blocks, slot, axis=0)
    return out.reshape((64 * piece.shape[0],) + piece.shape[1:])


def slice_product(matrix, gathered_piece):
    return complex_product(matrix, gathered_piece)


def local(exterior_rows, exterior_block, shared_block, crossing_block):
    start_rows = exterior_rows[0]
    own_exterior = exterior_block[0]
    own_shared = shared_block[0]
    own_crossing = crossing_block[0]
    width_panel = own_shared.shape[0]
    panel_index = lax.axis_index("panel")
    own_rows = lax.dynamic_slice_in_dim(start_rows, panel_index * width_panel, width_panel, 0)
    other_form, other_crossing = swapped((own_shared, own_crossing), "box", 0)

    def through_own(gathered_piece):
        return slice_product(own_shared, gathered_piece)

    def own_step(image_now):
        return own_rows + through_own(panel_gather(image_now))

    image_panel = complex_product(other_form, start_rows)
    rows_panel = own_step(image_panel)
    for iteration in range(1, ITERS):
        image_panel = slice_product(
            other_form, panel_gather(rows_panel)
        )
        rows_panel = own_step(image_panel)
    gathered_piece = panel_gather(rows_panel)
    image_final = slice_product(other_form, gathered_piece)
    other_terms = slice_product(other_crossing, gathered_piece)
    own_terms = slice_product(
        own_crossing, panel_gather(image_final)
    )
    merged = jnp.stack([own_exterior + own_terms, -other_terms], axis=0)
    return merged[None]


def solution(mesh):
    return jax.shard_map(
        local,
        mesh=mesh,
        in_specs=(
            P("box", None, None, None),
            P("box", "panel", None, None),
            P("box", "panel", None, None),
            P("box", "panel", None, None),
        ),
        out_specs=P("box", None, "panel", None, None),
        check_vma=False,
    )
```

```python
import jax
import jax.numpy as jnp
from jax import lax
from jax.sharding import PartitionSpec as P

ITERS = 3


def swapped(shard, axis, bit):
    return lax.ppermute(shard, axis, [(i, i ^ 1 << bit) for i in range(lax.axis_size(axis))])


def complex_product(left_factor, operand):
    highest = lax.Precision.HIGHEST
    real_part = jnp.dot(
        left_factor[:, 0], operand[:, 0], precision=highest, preferred_element_type=jnp.float32
    ) - jnp.dot(
        left_factor[:, 1], operand[:, 1], precision=highest, preferred_element_type=jnp.float32
    )
    imag_part = jnp.dot(
        left_factor[:, 0], operand[:, 1], precision=highest, preferred_element_type=jnp.float32
    ) + jnp.dot(
        left_factor[:, 1], operand[:, 0], precision=highest, preferred_element_type=jnp.float32
    )
    return jnp.stack([real_part, imag_part], axis=1)


def shifted_along(piece, stride, shift):
    pairs = []
    for source in range(lax.axis_size("panel")):
        own = (source // stride) % 4
        pairs.append((source, source + ((own + shift) % 4 - own) * stride))
    return lax.ppermute(piece, "panel", pairs)


def direct_stage(blocks, stride):
    return jnp.stack(
        [blocks, shifted_along(blocks, stride, 3), shifted_along(blocks, stride, 2),
         shifted_along(blocks, stride, 1)], 0)


def relay_stage(blocks, stride):
    from_below = shifted_along(blocks, stride, 1)
    from_above = shifted_along(blocks, stride, 3)
    half = blocks.shape[0] // 2
    opposite = jnp.concatenate(
        [shifted_along(from_below[:half], stride, 1), shifted_along(from_above[half:], stride, 3)], 0)
    return jnp.stack([blocks, from_above, opposite, from_below], 0)


def panel_gather(piece):
    blocks = direct_stage(piece[None], 1)
    blocks = direct_stage(blocks, 4)
    blocks = relay_stage(blocks, 16)
    blocks = blocks.reshape((64,) + piece.shape)
    me = lax.axis_index("panel")
    target = jnp.arange(64)
    slot = jnp.zeros((64,), jnp.int32)
    for stride in (16, 4, 1):
        offset = (target // stride % 4 - me // stride % 4) % 4
        slot = slot + offset * stride
    out = jnp.take(blocks, slot, axis=0, mode="clip")
    return out.reshape((64 * piece.shape[0],) + piece.shape[1:])


def slice_product(matrix, gathered_piece):
    return complex_product(matrix, gathered_piece)


def local(exterior_rows, exterior_block, shared_block, crossing_block):
    start_rows = exterior_rows[0]
    own_exterior = exterior_block[0]
    own_shared = shared_block[0]
    own_crossing = crossing_block[0]
    width_panel = own_shared.shape[0]
    panel_index = lax.axis_index("panel")
    own_rows = lax.dynamic_slice_in_dim(start_rows, panel_index * width_panel, width_panel, 0)
    other_form = swapped(own_shared, "box", 0)
    other_crossing = swapped(own_crossing, "box", 0)

    def through_own(gathered_piece):
        return slice_product(own_shared, gathered_piece)

    def own_step(image_now):
        return own_rows + through_own(panel_gather(image_now))

    image_panel = complex_product(other_form, start_rows)
    rows_panel = own_step(image_panel)
    for iteration in range(1, ITERS):
        image_panel = slice_product(
            other_form, panel_gather(rows_panel)
        )
        rows_panel = own_step(image_panel)
    gathered_piece = panel_gather(rows_panel)
    image_final = slice_product(other_form, gathered_piece)
    other_terms = slice_product(other_crossing, gathered_piece)
    own_terms = slice_product(
        own_crossing, panel_gather(image_final)
    )
    merged = jnp.stack([own_exterior + own_terms, -other_terms], axis=0)
    return merged[None]


def solution(mesh):
    return jax.shard_map(
        local,
        mesh=mesh,
        in_specs=(
            P("box", None, None, None),
            P("box", "panel", None, None),
            P("box", "panel", None, None),
            P("box", "panel", None, None),
        ),
        out_specs=P("box", None, "panel", None, None),
        check_vma=False,
    )
```

```python
import jax
import jax.numpy as jnp
from jax import lax
from jax.sharding import PartitionSpec as P

ITERS = 3


def swapped(shard, axis, bit):
    return lax.ppermute(shard, axis, [(i, i ^ 1 << bit) for i in range(lax.axis_size(axis))])


def complex_product(left_factor, operand):
    highest = lax.Precision.HIGHEST
    real_part = jnp.dot(
        left_factor[:, 0], operand[:, 0], precision=highest, preferred_element_type=jnp.float32
    ) - jnp.dot(
        left_factor[:, 1], operand[:, 1], precision=highest, preferred_element_type=jnp.float32
    )
    imag_part = jnp.dot(
        left_factor[:, 0], operand[:, 1], precision=highest, preferred_element_type=jnp.float32
    ) + jnp.dot(
        left_factor[:, 1], operand[:, 0], precision=highest, preferred_element_type=jnp.float32
    )
    return jnp.stack([real_part, imag_part], axis=1)


def shifted_along(piece, stride, shift):
    pairs = []
    for source in range(lax.axis_size("panel")):
        own = (source // stride) % 4
        pairs.append((source, source + ((own + shift) % 4 - own) * stride))
    return lax.ppermute(piece, "panel", pairs)


def direct_stage(blocks, stride):
    return jnp.stack(
        [blocks, shifted_along(blocks, stride, 3), shifted_along(blocks, stride, 2),
         shifted_along(blocks, stride, 1)], 0)


def relay_stage(blocks, stride, axis=0):
    from_below = shifted_along(blocks, stride, 1)
    from_above = shifted_along(blocks, stride, 3)
    half = blocks.shape[axis] // 2
    opposite = jnp.concatenate(
        [shifted_along(lax.slice_in_dim(from_below, 0, half, axis=axis), stride, 1),
         shifted_along(lax.slice_in_dim(from_above, half, blocks.shape[axis], axis=axis), stride, 3)],
        axis)
    return jnp.stack([blocks, from_above, opposite, from_below], 0)


def panel_gather(piece):
    blocks = relay_stage(piece[None], 1, axis=1)
    blocks = direct_stage(blocks, 4)
    blocks = relay_stage(blocks, 16)
    blocks = blocks.reshape((64,) + piece.shape)
    me = lax.axis_index("panel")
    target = jnp.arange(64)
    slot = jnp.zeros((64,), jnp.int32)
    for stride in (16, 4, 1):
        offset = (target // stride % 4 - me // stride % 4) % 4
        slot = slot + offset * stride
    out = jnp.take(blocks, slot, axis=0, mode="clip")
    return out.reshape((64 * piece.shape[0],) + piece.shape[1:])


def slice_product(matrix, gathered_piece):
    return complex_product(matrix, gathered_piece)


def local(exterior_rows, exterior_block, shared_block, crossing_block):
    start_rows = exterior_rows[0]
    own_exterior = exterior_block[0]
    own_shared = shared_block[0]
    own_crossing = crossing_block[0]
    width_panel = own_shared.shape[0]
    panel_index = lax.axis_index("panel")
    own_rows = lax.dynamic_slice_in_dim(start_rows, panel_index * width_panel, width_panel, 0)
    other_form = swapped(own_shared, "box", 0)
    other_crossing = swapped(own_crossing, "box", 0)

    def through_own(gathered_piece):
        return slice_product(own_shared, gathered_piece)

    def own_step(image_now):
        return own_rows + through_own(panel_gather(image_now))

    image_panel = complex_product(other_form, start_rows)
    rows_panel = own_step(image_panel)
    for iteration in range(1, ITERS):
        image_panel = slice_product(
            other_form, panel_gather(rows_panel)
        )
        rows_panel = own_step(image_panel)
    gathered_piece = panel_gather(rows_panel)
    image_final = slice_product(other_form, gathered_piece)
    other_terms = slice_product(other_crossing, gathered_piece)
    own_terms = slice_product(
        own_crossing, panel_gather(image_final)
    )
    merged = jnp.stack([own_exterior + own_terms, -other_terms], axis=0)
    return merged[None]


def solution(mesh):
    return jax.shard_map(
        local,
        mesh=mesh,
        in_specs=(
            P("box", None, None, None),
            P("box", "panel", None, None),
            P("box", "panel", None, None),
            P("box", "panel", None, None),
        ),
        out_specs=P("box", None, "panel", None, None),
        check_vma=False,
    )
```

```python
import jax
import jax.numpy as jnp
from jax import lax
from jax.sharding import PartitionSpec as P

ITERS = 3


def swapped(shard, axis, bit):
    return lax.ppermute(shard, axis, [(i, i ^ 1 << bit) for i in range(lax.axis_size(axis))])


def complex_product(left_factor, operand):
    highest = lax.Precision.HIGH
    real_part = jnp.dot(
        left_factor[:, 0], operand[:, 0], precision=highest, preferred_element_type=jnp.float32
    ) - jnp.dot(
        left_factor[:, 1], operand[:, 1], precision=highest, preferred_element_type=jnp.float32
    )
    imag_part = jnp.dot(
        left_factor[:, 0], operand[:, 1], precision=highest, preferred_element_type=jnp.float32
    ) + jnp.dot(
        left_factor[:, 1], operand[:, 0], precision=highest, preferred_element_type=jnp.float32
    )
    return jnp.stack([real_part, imag_part], axis=1)


def shifted_along(piece, stride, shift):
    pairs = []
    for source in range(lax.axis_size("panel")):
        own = (source // stride) % 4
        pairs.append((source, source + ((own + shift) % 4 - own) * stride))
    return lax.ppermute(piece, "panel", pairs)


def direct_stage(blocks, stride):
    return jnp.stack(
        [blocks, shifted_along(blocks, stride, 3), shifted_along(blocks, stride, 2),
         shifted_along(blocks, stride, 1)], 0)


def relay_stage(blocks, stride):
    from_below = shifted_along(blocks, stride, 1)
    from_above = shifted_along(blocks, stride, 3)
    half = blocks.shape[0] // 2
    opposite = jnp.concatenate(
        [shifted_along(from_below[:half], stride, 1), shifted_along(from_above[half:], stride, 3)], 0)
    return jnp.stack([blocks, from_above, opposite, from_below], 0)


def panel_gather(piece):
    blocks = direct_stage(piece[None], 1)
    blocks = direct_stage(blocks, 4)
    blocks = relay_stage(blocks, 16)
    blocks = blocks.reshape((64,) + piece.shape)
    me = lax.axis_index("panel")
    target = jnp.arange(64)
    slot = jnp.zeros((64,), jnp.int32)
    for stride in (16, 4, 1):
        offset = (target // stride % 4 - me // stride % 4) % 4
        slot = slot + offset * stride
    out = jnp.take(blocks, slot, axis=0, mode="clip")
    return out.reshape((64 * piece.shape[0],) + piece.shape[1:])


def slice_product(matrix, gathered_piece):
    return complex_product(matrix, gathered_piece)


def local(exterior_rows, exterior_block, shared_block, crossing_block):
    start_rows = exterior_rows[0]
    own_exterior = exterior_block[0]
    own_shared = shared_block[0]
    own_crossing = crossing_block[0]
    width_panel = own_shared.shape[0]
    panel_index = lax.axis_index("panel")
    own_rows = lax.dynamic_slice_in_dim(start_rows, panel_index * width_panel, width_panel, 0)
    other_form = swapped(own_shared, "box", 0)
    other_crossing = swapped(own_crossing, "box", 0)

    def through_own(gathered_piece):
        return slice_product(own_shared, gathered_piece)

    def own_step(image_now):
        return own_rows + through_own(panel_gather(image_now))

    image_panel = complex_product(other_form, start_rows)
    rows_panel = own_step(image_panel)
    for iteration in range(1, ITERS):
        image_panel = slice_product(
            other_form, panel_gather(rows_panel)
        )
        rows_panel = own_step(image_panel)
    gathered_piece = panel_gather(rows_panel)
    image_final = slice_product(other_form, gathered_piece)
    other_terms = slice_product(other_crossing, gathered_piece)
    own_terms = slice_product(
        own_crossing, panel_gather(image_final)
    )
    merged = jnp.stack([own_exterior + own_terms, -other_terms], axis=0)
    return merged[None]


def solution(mesh):
    return jax.shard_map(
        local,
        mesh=mesh,
        in_specs=(
            P("box", None, None, None),
            P("box", "panel", None, None),
            P("box", "panel", None, None),
            P("box", "panel", None, None),
        ),
        out_specs=P("box", None, "panel", None, None),
        check_vma=False,
    )
```

```python
import jax
import jax.numpy as jnp
from jax import lax
from jax.sharding import PartitionSpec as P

ITERS = 3


def swapped(shard, axis, bit):
    return lax.ppermute(shard, axis, [(i, i ^ 1 << bit) for i in range(lax.axis_size(axis))])


def complex_product(left_factor, operand):
    highest = lax.Precision.HIGH
    real_part = jnp.dot(
        left_factor[:, 0], operand[:, 0], precision=highest, preferred_element_type=jnp.float32
    ) - jnp.dot(
        left_factor[:, 1], operand[:, 1], precision=highest, preferred_element_type=jnp.float32
    )
    imag_part = jnp.dot(
        left_factor[:, 0], operand[:, 1], precision=highest, preferred_element_type=jnp.float32
    ) + jnp.dot(
        left_factor[:, 1], operand[:, 0], precision=highest, preferred_element_type=jnp.float32
    )
    return jnp.stack([real_part, imag_part], axis=1)


def shifted_along(piece, stride, shift):
    pairs = []
    for source in range(lax.axis_size("panel")):
        own = (source // stride) % 4
        pairs.append((source, source + ((own + shift) % 4 - own) * stride))
    return lax.ppermute(piece, "panel", pairs)


def direct_stage(blocks, stride):
    return jnp.stack(
        [blocks, shifted_along(blocks, stride, 3), shifted_along(blocks, stride, 2),
         shifted_along(blocks, stride, 1)], 0)


def relay_stage(blocks, stride):
    from_below = shifted_along(blocks, stride, 1)
    from_above = shifted_along(blocks, stride, 3)
    half = blocks.shape[0] // 2
    opposite = jnp.concatenate(
        [shifted_along(from_below[:half], stride, 1), shifted_along(from_above[half:], stride, 3)], 0)
    return jnp.stack([blocks, from_above, opposite, from_below], 0)


def panel_gather(piece):
    blocks = direct_stage(piece[None], 1)
    blocks = direct_stage(blocks, 4)
    blocks = relay_stage(blocks, 16)
    blocks = blocks.reshape((64,) + piece.shape)
    me = lax.axis_index("panel")
    target = jnp.arange(64)
    slot = jnp.zeros((64,), jnp.int32)
    for stride in (16, 4, 1):
        offset = (target // stride % 4 - me // stride % 4) % 4
        slot = slot + offset * stride
    out = jnp.take(blocks, slot, axis=0, mode="clip")
    return out.reshape((64 * piece.shape[0],) + piece.shape[1:])


def slice_product(matrix, gathered_piece):
    return complex_product(matrix, gathered_piece)


def local(exterior_rows, exterior_block, shared_block, crossing_block):
    start_rows = exterior_rows[0]
    own_exterior = exterior_block[0]
    own_shared = shared_block[0]
    own_crossing = crossing_block[0]
    width_panel = own_shared.shape[0]
    panel_index = lax.axis_index("panel")
    own_rows = lax.dynamic_slice_in_dim(start_rows, panel_index * width_panel, width_panel, 0)
    other_form = swapped(own_shared, "box", 0)
    other_crossing = swapped(own_crossing, "box", 0)

    blocks_by_parity = jnp.stack([own_shared, other_form], 0)

    def step(index, vector):
        parity = index % 2
        matrix = lax.dynamic_index_in_dim(blocks_by_parity, parity, 0, keepdims=False)
        addend = own_rows * (1 - parity).astype(own_rows.dtype)
        return addend + slice_product(matrix, panel_gather(vector))

    image_panel = complex_product(other_form, start_rows)
    rows_panel = lax.fori_loop(0, 2 * ITERS - 1, step, image_panel)
    gathered_piece = panel_gather(rows_panel)
    image_final = slice_product(other_form, gathered_piece)
    other_terms = slice_product(other_crossing, gathered_piece)
    own_terms = slice_product(
        own_crossing, panel_gather(image_final)
    )
    merged = jnp.stack([own_exterior + own_terms, -other_terms], axis=0)
    return merged[None]


def solution(mesh):
    return jax.shard_map(
        local,
        mesh=mesh,
        in_specs=(
            P("box", None, None, None),
            P("box", "panel", None, None),
            P("box", "panel", None, None),
            P("box", "panel", None, None),
        ),
        out_specs=P("box", None, "panel", None, None),
        check_vma=False,
    )
```

```python
import jax
import jax.numpy as jnp
from jax import lax
from jax.sharding import PartitionSpec as P

ITERS = 3


def swapped(shard, axis, bit):
    return lax.ppermute(shard, axis, [(i, i ^ 1 << bit) for i in range(lax.axis_size(axis))])


def complex_product(left_factor, operand):
    highest = lax.Precision.HIGH
    real_part = jnp.dot(
        left_factor[:, 0], operand[:, 0], precision=highest, preferred_element_type=jnp.float32
    ) - jnp.dot(
        left_factor[:, 1], operand[:, 1], precision=highest, preferred_element_type=jnp.float32
    )
    imag_part = jnp.dot(
        left_factor[:, 0], operand[:, 1], precision=highest, preferred_element_type=jnp.float32
    ) + jnp.dot(
        left_factor[:, 1], operand[:, 0], precision=highest, preferred_element_type=jnp.float32
    )
    return jnp.stack([real_part, imag_part], axis=1)


def shifted_along(piece, stride, shift):
    pairs = []
    for source in range(lax.axis_size("panel")):
        own = (source // stride) % 4
        pairs.append((source, source + ((own + shift) % 4 - own) * stride))
    return lax.ppermute(piece, "panel", pairs)


def direct_stage(blocks, stride):
    return jnp.stack(
        [blocks, shifted_along(blocks, stride, 3), shifted_along(blocks, stride, 2),
         shifted_along(blocks, stride, 1)], 0)


def relay_stage(blocks, stride):
    from_below = shifted_along(blocks, stride, 1)
    from_above = shifted_along(blocks, stride, 3)
    half = blocks.shape[0] // 2
    opposite = jnp.concatenate(
        [shifted_along(from_below[:half], stride, 1), shifted_along(from_above[half:], stride, 3)], 0)
    return jnp.stack([blocks, from_above, opposite, from_below], 0)


def panel_gather(piece):
    planar = jnp.swapaxes(piece, 0, 1)
    blocks = direct_stage(planar[None], 1)
    blocks = direct_stage(blocks, 4)
    blocks = relay_stage(blocks, 16)
    blocks = jnp.swapaxes(blocks.reshape((64,) + planar.shape), 0, 1)
    me = lax.axis_index("panel")
    target = jnp.arange(64)
    slot = jnp.zeros((64,), jnp.int32)
    for stride in (16, 4, 1):
        offset = (target // stride % 4 - me // stride % 4) % 4
        slot = slot + offset * stride
    out = jnp.take(blocks, slot, axis=1, mode="clip")
    return out.reshape((2, 64 * piece.shape[0], piece.shape[2]))


def slice_product(matrix, gathered_piece):
    highest = lax.Precision.HIGH
    real_part = jnp.dot(
        matrix[:, 0], gathered_piece[0], precision=highest, preferred_element_type=jnp.float32
    ) - jnp.dot(
        matrix[:, 1], gathered_piece[1], precision=highest, preferred_element_type=jnp.float32
    )
    imag_part = jnp.dot(
        matrix[:, 0], gathered_piece[1], precision=highest, preferred_element_type=jnp.float32
    ) + jnp.dot(
        matrix[:, 1], gathered_piece[0], precision=highest, preferred_element_type=jnp.float32
    )
    return jnp.stack([real_part, imag_part], axis=1)


def local(exterior_rows, exterior_block, shared_block, crossing_block):
    start_rows = exterior_rows[0]
    own_exterior = exterior_block[0]
    own_shared = shared_block[0]
    own_crossing = crossing_block[0]
    width_panel = own_shared.shape[0]
    panel_index = lax.axis_index("panel")
    own_rows = lax.dynamic_slice_in_dim(start_rows, panel_index * width_panel, width_panel, 0)
    other_form = swapped(own_shared, "box", 0)
    other_crossing = swapped(own_crossing, "box", 0)

    def through_own(gathered_piece):
        return slice_product(own_shared, gathered_piece)

    def own_step(image_now):
        return own_rows + through_own(panel_gather(image_now))

    image_panel = complex_product(other_form, start_rows)
    rows_panel = own_step(image_panel)
    for iteration in range(1, ITERS):
        image_panel = slice_product(
            other_form, panel_gather(rows_panel)
        )
        rows_panel = own_step(image_panel)
    gathered_piece = panel_gather(rows_panel)
    image_final = slice_product(other_form, gathered_piece)
    other_terms = slice_product(other_crossing, gathered_piece)
    own_terms = slice_product(
        own_crossing, panel_gather(image_final)
    )
    merged = jnp.stack([own_exterior + own_terms, -other_terms], axis=0)
    return merged[None]


def solution(mesh):
    return jax.shard_map(
        local,
        mesh=mesh,
        in_specs=(
            P("box", None, None, None),
            P("box", "panel", None, None),
            P("box", "panel", None, None),
            P("box", "panel", None, None),
        ),
        out_specs=P("box", None, "panel", None, None),
        check_vma=False,
    )
```

```python
import jax
import jax.numpy as jnp
from jax import lax
from jax.sharding import PartitionSpec as P

ITERS = 3


def swapped(shard, axis, bit):
    return lax.ppermute(shard, axis, [(i, i ^ 1 << bit) for i in range(lax.axis_size(axis))])


def complex_product(left_factor, operand):
    highest = lax.Precision.HIGH
    real_part = jnp.dot(
        left_factor[:, 0], operand[:, 0], precision=highest, preferred_element_type=jnp.float32
    ) - jnp.dot(
        left_factor[:, 1], operand[:, 1], precision=highest, preferred_element_type=jnp.float32
    )
    imag_part = jnp.dot(
        left_factor[:, 0], operand[:, 1], precision=highest, preferred_element_type=jnp.float32
    ) + jnp.dot(
        left_factor[:, 1], operand[:, 0], precision=highest, preferred_element_type=jnp.float32
    )
    return jnp.stack([real_part, imag_part], axis=1)


def shifted_along(piece, stride, shift):
    pairs = []
    for source in range(lax.axis_size("panel")):
        own = (source // stride) % 4
        pairs.append((source, source + ((own + shift) % 4 - own) * stride))
    return lax.ppermute(piece, "panel", pairs)


def direct_stage(blocks, stride):
    return jnp.stack(
        [blocks, shifted_along(blocks, stride, 3), shifted_along(blocks, stride, 2),
         shifted_along(blocks, stride, 1)], 0)


def relay_stage(blocks, stride):
    from_below = shifted_along(blocks, stride, 1)
    from_above = shifted_along(blocks, stride, 3)
    half = blocks.shape[0] // 2
    opposite = jnp.concatenate(
        [shifted_along(from_below[:half], stride, 1), shifted_along(from_above[half:], stride, 3)], 0)
    return jnp.stack([blocks, from_above, opposite, from_below], 0)


def panel_gather(piece):
    planar = jnp.swapaxes(piece, 0, 1)
    blocks = direct_stage(planar[None], 1)
    blocks = direct_stage(blocks, 16)
    blocks = relay_stage(blocks, 4)
    blocks = jnp.swapaxes(blocks.reshape((64,) + planar.shape), 0, 1)
    me = lax.axis_index("panel")
    target = jnp.arange(64)
    slot = jnp.zeros((64,), jnp.int32)
    for stride, place in ((4, 16), (16, 4), (1, 1)):
        offset = (target // stride % 4 - me // stride % 4) % 4
        slot = slot + offset * place
    out = jnp.take(blocks, slot, axis=1, mode="clip")
    return out.reshape((2, 64 * piece.shape[0], piece.shape[2]))


def slice_product(matrix, gathered_piece):
    highest = lax.Precision.HIGH
    real_part = jnp.dot(
        matrix[:, 0], gathered_piece[0], precision=highest, preferred_element_type=jnp.float32
    ) - jnp.dot(
        matrix[:, 1], gathered_piece[1], precision=highest, preferred_element_type=jnp.float32
    )
    imag_part = jnp.dot(
        matrix[:, 0], gathered_piece[1], precision=highest, preferred_element_type=jnp.float32
    ) + jnp.dot(
        matrix[:, 1], gathered_piece[0], precision=highest, preferred_element_type=jnp.float32
    )
    return jnp.stack([real_part, imag_part], axis=1)


def local(exterior_rows, exterior_block, shared_block, crossing_block):
    start_rows = exterior_rows[0]
    own_exterior = exterior_block[0]
    own_shared = shared_block[0]
    own_crossing = crossing_block[0]
    width_panel = own_shared.shape[0]
    panel_index = lax.axis_index("panel")
    own_rows = lax.dynamic_slice_in_dim(start_rows, panel_index * width_panel, width_panel, 0)
    other_form = swapped(own_shared, "box", 0)
    other_crossing = swapped(own_crossing, "box", 0)

    def through_own(gathered_piece):
        return slice_product(own_shared, gathered_piece)

    def own_step(image_now):
        return own_rows + through_own(panel_gather(image_now))

    image_panel = complex_product(other_form, start_rows)
    rows_panel = own_step(image_panel)
    for iteration in range(1, ITERS):
        image_panel = slice_product(
            other_form, panel_gather(rows_panel)
        )
        rows_panel = own_step(image_panel)
    gathered_piece = panel_gather(rows_panel)
    image_final = slice_product(other_form, gathered_piece)
    other_terms = slice_product(other_crossing, gathered_piece)
    own_terms = slice_product(
        own_crossing, panel_gather(image_final)
    )
    merged = jnp.stack([own_exterior + own_terms, -other_terms], axis=0)
    return merged[None]


def solution(mesh):
    return jax.shard_map(
        local,
        mesh=mesh,
        in_specs=(
            P("box", None, None, None),
            P("box", "panel", None, None),
            P("box", "panel", None, None),
            P("box", "panel", None, None),
        ),
        out_specs=P("box", None, "panel", None, None),
        check_vma=False,
    )
```
